512 devices in a mesh: row: 32 (over z_lo, x), col: 16 (over y, z_hi, core).
Axes of the slice: x: 4, y: 4, z: 16 (z_hi: 2, z_lo: 8; z = z_hi * 8 + z_lo), core: 2. Of those that a mesh axis runs over, the one named last changes fastest.
Arguments:
- anc_inv: bfloat16 [16384, 16384], P('row', 'col'), may hold values from -0.0546875 to 0.0546875
- panel: bfloat16 [1, 12288, 2048], P(None, 'col', 'row'), may hold values from -6 to 6
- structure: int32 [1, 96], replicated, may hold values from 0 to 127, as said below
Outputs:
- off_inv: float32 [1, 16384, 2048], P(None, 'row', 'col')
The draws below stay inside these ranges and needn't reach their ends.
Inputs may be any that keep to these rules, and one draw needn't show every extreme that they name: Each structure[s] holds 96 distinct ancestor block indices, in the order in which the panel stores its row blocks (not sorted); each group of 8 consecutive ancestor blocks holds 5 to 7 of them, and some group of each supernode holds exactly 7.
All inputs are finite; a program needn't handle non-finite values.
Results may differ from the reference program's by a relative error of at most 0.0003.
Values may be sent and summed in bfloat16 or wider, within the bound.
No kernel may reach another device: no remote copies, remote signals or barrier semaphores. Data moves between devices by JAX's collectives and lax.ppermute only.
A program may use at most 64 MiB of HBM per device.

```python
import jax
import jax.numpy as jnp
from jax import lax

BS = 128
W = 2048
SBLK = 96
NAB = 128
NSUP = 1
NA = 16384
SROWS = 12288
GROUP = 8
CAP = 7
N_COL = 16


def draw_structure(key, part):
    col_count = NAB // GROUP
    pair_count = col_count // 2
    mean_count = CAP - 1
    rows_out = []
    for supernode in range(NSUP):
        sub_key = jax.random.fold_in(key, 101 + supernode)
        key_pairs, key_first, key_order, key_ranks, key_shuffle = jax.random.split(sub_key, 5)
        choose = jax.random.randint(key_pairs, (pair_count,), 0, 3)
        forced = jax.random.randint(key_first, (1,), 0, 2) * 2
        choose = jnp.concatenate([forced, choose[1:]])
        counts = jnp.stack([mean_count - 1 + choose, mean_count + 1 - choose], axis=1).reshape(col_count)
        counts = jax.random.permutation(key_order, counts)
        ordinal = jax.vmap(lambda branch_key: jax.random.permutation(branch_key, GROUP))(jax.random.split(key_ranks, col_count))
        chosen = (ordinal < counts[:, None]).reshape(NAB)
        scores = jnp.where(chosen, 0, NAB) + jnp.arange(NAB, dtype=jnp.int32)
        ordering = jnp.argsort(scores, stable=True)[:SBLK].astype(jnp.int32)
        shuffled = jax.random.permutation(key_shuffle, ordering)
        rows_out.append(shuffled.astype(jnp.int32))
    return jnp.stack(rows_out)


def shard_levels(own_key, shape, cuts, low, high):
    def one(dim, parts):
        steps = jax.random.uniform(jax.random.fold_in(jax.random.fold_in(own_key, 6), dim), (parts,), jnp.float32, low / len(cuts), high / len(cuts))
        return jnp.repeat(jnp.exp(steps), shape[dim] // parts).reshape((-1,) + (1,) * (len(shape) - dim - 1))

    gain = one(*cuts[0])
    for cut in cuts[1:]:
        gain = gain * one(*cut)
    return gain


def scatter_about(key, dims, scale, most, shards=(), held_as=jnp.bfloat16):
    factor_of = shard_levels(key, dims, shards, -0.22, 0.18) if shards else 1.0
    values = jax.random.normal(key, dims, jnp.float32) * scale * factor_of
    return jnp.minimum(jnp.maximum(values, -most), most).astype(held_as)


def setup_inputs(seed: int = 0) -> dict:
    arg_keys = jax.random.split(jax.random.key(seed), 4)
    return {
        "anc_inv": scatter_about(arg_keys[0], (NA, NA), SROWS ** -0.5, 0.0546875, ((0, 32), (1, 16))),
        "panel": scatter_about(arg_keys[1], (NSUP, SROWS, W), 1.0, 6.0, ((1, 16), (2, 32))),
        "structure": draw_structure(jax.random.fold_in(arg_keys[3], 71), 0),
    }


def reference(anc_inv, panel, structure):
    group_blocks = NAB // N_COL
    ancestors = jnp.arange(NAB, dtype=jnp.int32)
    results = []
    for supernode in range(NSUP):
        onehot = structure[supernode][None, :] == ancestors[:, None]
        compact = panel[supernode].astype(jnp.float32).reshape(SBLK, BS * W)
        expanded = jnp.dot(onehot.astype(jnp.float32), compact, precision=lax.Precision.HIGHEST).reshape(NAB * BS, W)

        def add_group(group_index, total):
            offset = (group_index * (group_blocks * BS)).astype(jnp.int32)
            columns = lax.dynamic_slice_in_dim(anc_inv, offset, group_blocks * BS, 1).astype(jnp.float32)
            rows_part = lax.dynamic_slice_in_dim(expanded, offset, group_blocks * BS, 0)
            partial_value = jnp.dot(columns, rows_part, precision=lax.Precision.HIGHEST)
            return total + partial_value

        total = lax.fori_loop(0, N_COL, add_group, jnp.zeros((NAB * BS, W), jnp.float32))
        member = jnp.repeat(jnp.any(onehot, axis=1), BS)
        results.append(jnp.where(member[:, None], -total, jnp.zeros_like(total)))
    return jnp.stack(results)
```

```python
import jax
import jax.numpy as jnp
from jax import lax
from jax.sharding import Mesh, PartitionSpec as P

BS = 128
SBLK = 96
ROW = ("zl", "x")
COL = ("y", "zh", "c")


def body(anc_inv, panel, structure):
    col_index = lax.axis_index(COL)
    row_index = lax.axis_index(ROW)
    local_rows, local_cols = anc_inv.shape
    group_blocks = local_cols // BS
    local_width = panel.shape[2]
    gathered = lax.all_gather(panel, COL, axis=1, tiled=True)
    own_blocks = row_index * (local_rows // BS) + jnp.arange(local_rows // BS, dtype=jnp.int32)
    block_ids = jnp.arange(group_blocks, dtype=jnp.int32)
    blocks_of = structure[0]
    compact = gathered[0].reshape(SBLK, BS * local_width)
    local_block = blocks_of - col_index * group_blocks
    picker = (local_block[None, :] == block_ids[:, None]).astype(jnp.bfloat16)
    picked = (
        jnp.dot(picker, compact, preferred_element_type=jnp.float32)
        .astype(jnp.bfloat16)
        .reshape(group_blocks * BS, local_width)
    )
    partial_value = jnp.dot(
        anc_inv,
        lax.all_gather(lax.all_gather(picked, "x", axis=1, tiled=True), "zl", axis=1, tiled=True),
        preferred_element_type=jnp.float32,
    )
    summed = lax.psum_scatter(partial_value, COL, scatter_dimension=1, tiled=True)
    member = jnp.any(blocks_of[None, :] == own_blocks[:, None], axis=1)
    row_mask = jnp.repeat(member, BS)
    results = [jnp.where(row_mask[:, None], -summed, jnp.zeros_like(summed))]
    return jnp.stack(results)


def solution(mesh):
    rows, cols = mesh.shape["row"], mesh.shape["col"]
    fine = Mesh(mesh.devices.reshape(rows // 4, 4, cols // 4, 2, 2), ("zl", "x", "y", "zh", "c"))
    in_specs = (P(ROW, COL), P(None, COL, ROW), P())
    out_specs = P(None, ROW, COL)
    return jax.shard_map(body, mesh=fine, in_specs=in_specs, out_specs=out_specs, check_vma=False)
```

```python
import jax
import jax.numpy as jnp
from jax import lax
from jax.sharding import Mesh, PartitionSpec as P

BS = 128
SBLK = 96
ROW = ("zl", "x")
COL = ("y", "zh", "c")


def body(anc_inv, panel, structure):
    n_y, n_zh, n_c = lax.axis_size("y"), lax.axis_size("zh"), lax.axis_size("c")
    col_index = lax.axis_index(COL)
    row_index = lax.axis_index(ROW)
    zh_index = lax.axis_index("zh")
    local_rows, local_cols = anc_inv.shape
    group_blocks = local_cols // BS
    local_width = panel.shape[2]
    per_dev = panel.shape[1] // BS
    gathered = lax.all_gather(panel[0], "zh", axis=0, tiled=True)
    gathered = lax.all_gather(gathered, ("y", "c"), axis=0, tiled=True)
    blocks_of = structure[0]
    blocks_gathered = blocks_of.reshape(n_y, n_zh, n_c, per_dev).transpose(0, 2, 1, 3).reshape(SBLK)
    own_blocks = row_index * (local_rows // BS) + jnp.arange(local_rows // BS, dtype=jnp.int32)
    block_ids = jnp.arange(group_blocks, dtype=jnp.int32)
    compact = gathered.reshape(SBLK, BS * local_width)
    local_block = blocks_gathered - col_index * group_blocks
    picker = (local_block[None, :] == block_ids[:, None]).astype(jnp.bfloat16)
    picked = (
        jnp.dot(picker, compact, preferred_element_type=jnp.float32)
        .astype(jnp.bfloat16)
        .reshape(group_blocks * BS, local_width)
    )
    expanded = lax.all_gather(lax.all_gather(picked, "x", axis=1, tiled=True), "zl", axis=1, tiled=True)
    width = expanded.shape[1]
    chunk = width // (n_y * n_zh * n_c)
    rhs = expanded.reshape(-1, n_y, n_zh, n_c, chunk)
    partial_value = jnp.einsum("mk,kyzcn->yczmn", anc_inv, rhs, preferred_element_type=jnp.float32)
    partial_value = partial_value.reshape(n_y * n_c, n_zh, local_rows, chunk)
    halves = lax.psum_scatter(partial_value, ("y", "c"), scatter_dimension=0, tiled=True)[0]
    mine = lax.dynamic_index_in_dim(halves, zh_index, 0, keepdims=False)
    other = lax.dynamic_index_in_dim(halves, 1 - zh_index, 0, keepdims=False)
    summed = mine + lax.ppermute(other, "zh", [(0, 1), (1, 0)])
    member = jnp.any(blocks_of[None, :] == own_blocks[:, None], axis=1)
    row_mask = jnp.repeat(member, BS)
    results = [jnp.where(row_mask[:, None], -summed, jnp.zeros_like(summed))]
    return jnp.stack(results)


def solution(mesh):
    rows, cols = mesh.shape["row"], mesh.shape["col"]
    fine = Mesh(mesh.devices.reshape(rows // 4, 4, cols // 4, 2, 2), ("zl", "x", "y", "zh", "c"))
    in_specs = (P(ROW, COL), P(None, COL, ROW), P())
    out_specs = P(None, ROW, COL)
    return jax.shard_map(body, mesh=fine, in_specs=in_specs, out_specs=out_specs, check_vma=False)
```

```python
import jax
import jax.numpy as jnp
from jax import lax
from jax.sharding import Mesh, PartitionSpec as P

BS = 128
SBLK = 96
CAP = 7
ROW = ("zl", "x")
COL = ("y", "zh", "c")


def body(anc_inv, panel, structure):
    n_y, n_zh, n_c = lax.axis_size("y"), lax.axis_size("zh"), lax.axis_size("c")
    col_index = lax.axis_index(COL)
    row_index = lax.axis_index(ROW)
    zh_index = lax.axis_index("zh")
    local_rows, local_cols = anc_inv.shape
    group_blocks = local_cols // BS
    local_width = panel.shape[2]
    per_dev = panel.shape[1] // BS
    gathered = lax.all_gather(panel[0], "zh", axis=0, tiled=True)
    gathered = lax.all_gather(gathered, ("y", "c"), axis=0, tiled=True)
    blocks_of = structure[0]
    blocks_gathered = blocks_of.reshape(n_y, n_zh, n_c, per_dev).transpose(0, 2, 1, 3).reshape(SBLK)
    own_blocks = row_index * (local_rows // BS) + jnp.arange(local_rows // BS, dtype=jnp.int32)
    block_ids = jnp.arange(group_blocks, dtype=jnp.int32)
    compact = gathered.reshape(SBLK, BS * local_width)
    local_block = blocks_gathered - col_index * group_blocks
    hits = local_block[None, :] == block_ids[:, None]
    present = jnp.any(hits, axis=1)
    rank = jnp.cumsum(present.astype(jnp.int32)) - 1
    slot_ids = jnp.arange(CAP, dtype=jnp.int32)
    slot_of = present[None, :] & (rank[None, :] == slot_ids[:, None])
    picker = jnp.dot(slot_of.astype(jnp.float32), hits.astype(jnp.float32)).astype(jnp.bfloat16)
    slot_block = jnp.sum(jnp.where(slot_of, block_ids[None, :], 0), axis=1)
    picked = (
        jnp.dot(picker, compact, preferred_element_type=jnp.float32)
        .astype(jnp.bfloat16)
        .reshape(CAP * BS, local_width)
    )
    anc_kept = jnp.take(anc_inv.reshape(local_rows, group_blocks, BS), slot_block, axis=1).reshape(local_rows, CAP * BS)
    expanded = lax.all_gather(lax.all_gather(picked, "x", axis=1, tiled=True), "zl", axis=1, tiled=True)
    width = expanded.shape[1]
    chunk = width // (n_y * n_zh * n_c)
    rhs = expanded.reshape(-1, n_y, n_zh, n_c, chunk)
    partial_value = jnp.einsum("mk,kyzcn->yczmn", anc_kept, rhs, preferred_element_type=jnp.float32)
    partial_value = partial_value.reshape(n_y * n_c, n_zh, local_rows, chunk)
    halves = lax.psum_scatter(partial_value, ("y", "c"), scatter_dimension=0, tiled=True)[0]
    mine = lax.dynamic_index_in_dim(halves, zh_index, 0, keepdims=False)
    other = lax.dynamic_index_in_dim(halves, 1 - zh_index, 0, keepdims=False)
    summed = mine + lax.ppermute(other, "zh", [(0, 1), (1, 0)])
    member = jnp.any(blocks_of[None, :] == own_blocks[:, None], axis=1)
    row_mask = jnp.repeat(member, BS)
    results = [jnp.where(row_mask[:, None], -summed, jnp.zeros_like(summed))]
    return jnp.stack(results)


def solution(mesh):
    rows, cols = mesh.shape["row"], mesh.shape["col"]
    fine = Mesh(mesh.devices.reshape(rows // 4, 4, cols // 4, 2, 2), ("zl", "x", "y", "zh", "c"))
    in_specs = (P(ROW, COL), P(None, COL, ROW), P())
    out_specs = P(None, ROW, COL)
    return jax.shard_map(body, mesh=fine, in_specs=in_specs, out_specs=out_specs, check_vma=False)
```

```python
import jax
import jax.numpy as jnp
from jax import lax
from jax.sharding import Mesh, PartitionSpec as P

BS = 128
SBLK = 96
CAP = 7
SPLIT = 2
ROW = ("zl", "x")
COL = ("y", "zh", "c")


def body(anc_inv, panel, structure):
    n_y, n_zh, n_c = lax.axis_size("y"), lax.axis_size("zh"), lax.axis_size("c")
    col_index = lax.axis_index(COL)
    row_index = lax.axis_index(ROW)
    zh_index = lax.axis_index("zh")
    local_rows, local_cols = anc_inv.shape
    group_blocks = local_cols // BS
    local_width = panel.shape[2]
    per_dev = panel.shape[1] // BS
    gathered = lax.all_gather(panel[0], "zh", axis=0, tiled=True)
    gathered = lax.all_gather(gathered, ("y", "c"), axis=0, tiled=True)
    blocks_of = structure[0]
    blocks_gathered = blocks_of.reshape(n_y, n_zh, n_c, per_dev).transpose(0, 2, 1, 3).reshape(SBLK)
    own_blocks = row_index * (local_rows // BS) + jnp.arange(local_rows // BS, dtype=jnp.int32)
    block_ids = jnp.arange(group_blocks, dtype=jnp.int32)
    compact = gathered.reshape(SBLK, BS * local_width)
    local_block = blocks_gathered - col_index * group_blocks
    hits = local_block[None, :] == block_ids[:, None]
    present = jnp.any(hits, axis=1)
    rank = jnp.cumsum(present.astype(jnp.int32)) - 1
    slot_ids = jnp.arange(CAP, dtype=jnp.int32)
    slot_of = present[None, :] & (rank[None, :] == slot_ids[:, None])
    picker = jnp.dot(slot_of.astype(jnp.float32), hits.astype(jnp.float32)).astype(jnp.bfloat16)
    slot_block = jnp.sum(jnp.where(slot_of, block_ids[None, :], 0), axis=1)
    picked = (
        jnp.dot(picker, compact, preferred_element_type=jnp.float32)
        .astype(jnp.bfloat16)
        .reshape(CAP * BS, local_width)
    )
    anc_kept = jnp.take(anc_inv.reshape(local_rows, group_blocks, BS), slot_block, axis=1).reshape(local_rows, CAP * BS)
    expanded = lax.all_gather(lax.all_gather(picked, "x", axis=1, tiled=True), "zl", axis=1, tiled=True)
    width = expanded.shape[1]
    chunk = width // (n_y * n_zh * n_c)
    rhs = expanded.reshape(-1, n_y, n_zh, n_c, chunk)
    partial_value = jnp.einsum("mk,kyzcn->yczmn", anc_kept, rhs, preferred_element_type=jnp.float32)
    partial_value = partial_value.reshape(n_y * n_c, n_zh, local_rows, chunk)
    pieces = []
    step = local_rows // SPLIT
    for piece in range(SPLIT):
        part = partial_value[:, :, piece * step:(piece + 1) * step]
        halves = lax.psum_scatter(part, ("y", "c"), scatter_dimension=0, tiled=True)[0]
        mine = lax.dynamic_index_in_dim(halves, zh_index, 0, keepdims=False)
        other = lax.dynamic_index_in_dim(halves, 1 - zh_index, 0, keepdims=False)
        pieces.append(mine + lax.ppermute(other, "zh", [(0, 1), (1, 0)]))
    summed = jnp.concatenate(pieces, axis=0)
    member = jnp.any(blocks_of[None, :] == own_blocks[:, None], axis=1)
    row_mask = jnp.repeat(member, BS)
    results = [jnp.where(row_mask[:, None], -summed, jnp.zeros_like(summed))]
    return jnp.stack(results)


def solution(mesh):
    rows, cols = mesh.shape["row"], mesh.shape["col"]
    fine = Mesh(mesh.devices.reshape(rows // 4, 4, cols // 4, 2, 2), ("zl", "x", "y", "zh", "c"))
    in_specs = (P(ROW, COL), P(None, COL, ROW), P())
    out_specs = P(None, ROW, COL)
    return jax.shard_map(body, mesh=fine, in_specs=in_specs, out_specs=out_specs, check_vma=False)
```

```python
import jax
import jax.numpy as jnp
from jax import lax
from jax.sharding import Mesh, PartitionSpec as P

BS = 128
SBLK = 96
CAP = 7
ROW = ("zl", "x")
COL = ("y", "zh", "c")


def line_gather(v, axis, n):
    i = lax.axis_index(axis)
    right = [(j, j + 1) for j in range(n - 1)]
    left = [(j + 1, j) for j in range(n - 1)]
    from_left, from_right = [v], [v]
    a = b = v
    for _ in range(1, n):
        a = lax.ppermute(a, axis, right)
        b = lax.ppermute(b, axis, left)
        from_left.append(a)
        from_right.append(b)
    j = jnp.arange(n)
    got_left = jnp.take(jnp.stack(from_left), jnp.clip(i - j, 0, n - 1), axis=0)
    got_right = jnp.take(jnp.stack(from_right), jnp.clip(j - i, 0, n - 1), axis=0)
    return jnp.where((j <= i).reshape((n,) + (1,) * v.ndim), got_left, got_right)


def ring_gather(w, axis, n):
    i = lax.axis_index(axis)
    fwd = [(j, (j + 1) % n) for j in range(n)]
    bwd = [(j, (j - 1) % n) for j in range(n)]
    a = lax.ppermute(w, axis, fwd)
    b = lax.ppermute(w, axis, bwd)
    h = w.shape[0] // 2
    far = jnp.concatenate([lax.ppermute(a[:h], axis, fwd), lax.ppermute(b[h:], axis, bwd)])
    by_offset = jnp.stack([w, a, far, b])
    return jnp.take(by_offset, (i - jnp.arange(n)) % n, axis=0)


def body(anc_inv, panel, structure):
    n_y, n_zh, n_c = lax.axis_size("y"), lax.axis_size("zh"), lax.axis_size("c")
    col_index = lax.axis_index(COL)
    row_index = lax.axis_index(ROW)
    zh_index = lax.axis_index("zh")
    local_rows, local_cols = anc_inv.shape
    group_blocks = local_cols // BS
    local_width = panel.shape[2]
    per_dev = panel.shape[1] // BS
    gathered = lax.all_gather(panel[0], "zh", axis=0, tiled=True)
    gathered = lax.all_gather(gathered, ("y", "c"), axis=0, tiled=True)
    blocks_of = structure[0]
    blocks_gathered = blocks_of.reshape(n_y, n_zh, n_c, per_dev).transpose(0, 2, 1, 3).reshape(SBLK)
    own_blocks = row_index * (local_rows // BS) + jnp.arange(local_rows // BS, dtype=jnp.int32)
    block_ids = jnp.arange(group_blocks, dtype=jnp.int32)
    compact = gathered.reshape(SBLK, BS * local_width)
    local_block = blocks_gathered - col_index * group_blocks
    hits = local_block[None, :] == block_ids[:, None]
    present = jnp.any(hits, axis=1)
    rank = jnp.cumsum(present.astype(jnp.int32)) - 1
    slot_ids = jnp.arange(CAP, dtype=jnp.int32)
    slot_of = present[None, :] & (rank[None, :] == slot_ids[:, None])
    picker = jnp.dot(slot_of.astype(jnp.float32), hits.astype(jnp.float32)).astype(jnp.bfloat16)
    slot_block = jnp.sum(jnp.where(slot_of, block_ids[None, :], 0), axis=1)
    picked = (
        jnp.dot(picker, compact, preferred_element_type=jnp.float32)
        .astype(jnp.bfloat16)
        .reshape(CAP * BS, local_width)
    )
    anc_kept = jnp.take(anc_inv.reshape(local_rows, group_blocks, BS), slot_block, axis=1).reshape(local_rows, CAP * BS)
    n_zl, n_x = lax.axis_size("zl"), lax.axis_size("x")
    pieces = ring_gather(line_gather(picked, "zl", n_zl), "x", n_x)
    rhs = pieces.reshape(n_c, n_x // n_c, n_y, n_zh, CAP * BS, local_width)
    partial_value = jnp.einsum("mk,cxyzkn->yczmxn", anc_kept, rhs, preferred_element_type=jnp.float32)
    partial_value = partial_value.reshape(n_y * n_c, n_zh, local_rows, -1)
    halves = lax.psum_scatter(partial_value, ("y", "c"), scatter_dimension=0, tiled=True)[0]
    mine = lax.dynamic_index_in_dim(halves, zh_index, 0, keepdims=False)
    other = lax.dynamic_index_in_dim(halves, 1 - zh_index, 0, keepdims=False)
    summed = mine + lax.ppermute(other, "zh", [(0, 1), (1, 0)])
    member = jnp.any(blocks_of[None, :] == own_blocks[:, None], axis=1)
    row_mask = jnp.repeat(member, BS)
    results = [jnp.where(row_mask[:, None], -summed, jnp.zeros_like(summed))]
    return jnp.stack(results)


def solution(mesh):
    rows, cols = mesh.shape["row"], mesh.shape["col"]
    fine = Mesh(mesh.devices.reshape(rows // 4, 4, cols // 4, 2, 2), ("zl", "x", "y", "zh", "c"))
    in_specs = (P(ROW, COL), P(None, COL, ROW), P())
    out_specs = P(None, ROW, COL)
    return jax.shard_map(body, mesh=fine, in_specs=in_specs, out_specs=out_specs, check_vma=False)
```

```python
import jax
import jax.numpy as jnp
from jax import lax
from jax.sharding import Mesh, PartitionSpec as P

BS = 128
SBLK = 96
CAP = 7
ROW = ("zl", "x")
COL = ("y", "zh", "c")


def body(anc_inv, panel, structure):
    n_y, n_zh, n_c = lax.axis_size("y"), lax.axis_size("zh"), lax.axis_size("c")
    col_index = lax.axis_index(COL)
    row_index = lax.axis_index(ROW)
    zh_index = lax.axis_index("zh")
    local_rows, local_cols = anc_inv.shape
    group_blocks = local_cols // BS
    local_width = panel.shape[2]
    per_dev = panel.shape[1] // BS
    y_index, c_index = lax.axis_index("y"), lax.axis_index("c")
    blocks_of = structure[0]
    own_blocks = row_index * (local_rows // BS) + jnp.arange(local_rows // BS, dtype=jnp.int32)
    block_ids = jnp.arange(group_blocks, dtype=jnp.int32)
    held = lax.all_gather(panel[0], "zh", axis=0, tiled=True).reshape(n_zh * per_dev, BS * local_width)
    by_col = blocks_of.reshape(n_y, n_zh, n_c, per_dev)
    held_blocks = lax.dynamic_index_in_dim(lax.dynamic_index_in_dim(by_col, y_index, 0, False), c_index, 1, False)
    held_blocks = held_blocks.reshape(n_zh * per_dev)
    same_group = (held_blocks[:, None] // group_blocks) == (blocks_of[None, :] // group_blocks)
    slot = jnp.sum(same_group & (blocks_of[None, :] < held_blocks[:, None]), axis=1)
    dest_y = jnp.arange(n_y, dtype=jnp.int32)[:, None]
    dest_c = jnp.arange(n_c, dtype=jnp.int32)[None, :]
    dest_col = ((dest_y * n_zh + zh_index) * n_c + dest_c).reshape(n_y * n_c)
    slot_ids = jnp.arange(CAP, dtype=jnp.int32)
    placer = (
        ((held_blocks // group_blocks)[None, None, :] == dest_col[:, None, None])
        & (slot[None, None, :] == slot_ids[None, :, None])
    ).astype(jnp.bfloat16)
    placed = jnp.einsum("djq,qf->djf", placer, held, preferred_element_type=jnp.float32).astype(jnp.bfloat16)
    picked = lax.psum_scatter(placed, ("y", "c"), scatter_dimension=0, tiled=True)[0]
    picked = picked.reshape(CAP * BS, local_width)
    local_block = blocks_of - col_index * group_blocks
    hits = local_block[None, :] == block_ids[:, None]
    present = jnp.any(hits, axis=1)
    rank = jnp.cumsum(present.astype(jnp.int32)) - 1
    slot_of = present[None, :] & (rank[None, :] == slot_ids[:, None])
    slot_block = jnp.sum(jnp.where(slot_of, block_ids[None, :], 0), axis=1)
    anc_kept = jnp.take(anc_inv.reshape(local_rows, group_blocks, BS), slot_block, axis=1).reshape(local_rows, CAP * BS)
    expanded = lax.all_gather(lax.all_gather(picked, "x", axis=1, tiled=True), "zl", axis=1, tiled=True)
    width = expanded.shape[1]
    chunk = width // (n_y * n_zh * n_c)
    rhs = expanded.reshape(-1, n_y, n_zh, n_c, chunk)
    partial_value = jnp.einsum("mk,kyzcn->yczmn", anc_kept, rhs, preferred_element_type=jnp.float32)
    partial_value = partial_value.reshape(n_y * n_c, n_zh, local_rows, chunk)
    halves = lax.psum_scatter(partial_value, ("y", "c"), scatter_dimension=0, tiled=True)[0]
    mine = lax.dynamic_index_in_dim(halves, zh_index, 0, keepdims=False)
    other = lax.dynamic_index_in_dim(halves, 1 - zh_index, 0, keepdims=False)
    summed = mine + lax.ppermute(other, "zh", [(0, 1), (1, 0)])
    member = jnp.any(blocks_of[None, :] == own_blocks[:, None], axis=1)
    row_mask = jnp.repeat(member, BS)
    results = [jnp.where(row_mask[:, None], -summed, jnp.zeros_like(summed))]
    return jnp.stack(results)


def solution(mesh):
    rows, cols = mesh.shape["row"], mesh.shape["col"]
    fine = Mesh(mesh.devices.reshape(rows // 4, 4, cols // 4, 2, 2), ("zl", "x", "y", "zh", "c"))
    in_specs = (P(ROW, COL), P(None, COL, ROW), P())
    out_specs = P(None, ROW, COL)
    return jax.shard_map(body, mesh=fine, in_specs=in_specs, out_specs=out_specs, check_vma=False)
```

```python
import jax
import jax.numpy as jnp
from jax import lax
from jax.sharding import Mesh, PartitionSpec as P

BS = 128
SBLK = 96
CAP = 7
ROW = ("zl", "x")
COL = ("y", "zh", "c")


def body(anc_inv, panel, structure):
    n_y, n_zh, n_c = lax.axis_size("y"), lax.axis_size("zh"), lax.axis_size("c")
    col_index = lax.axis_index(COL)
    row_index = lax.axis_index(ROW)
    zh_index = lax.axis_index("zh")
    local_rows, local_cols = anc_inv.shape
    group_blocks = local_cols // BS
    local_width = panel.shape[2]
    per_dev = panel.shape[1] // BS
    lanes = BS
    dense = panel[0].reshape(-1, lanes)
    gathered = lax.all_gather(dense, "zh", axis=0, tiled=True)
    gathered = lax.all_gather(gathered, ("y", "c"), axis=0, tiled=True)
    blocks_of = structure[0]
    blocks_gathered = blocks_of.reshape(n_y, n_zh, n_c, per_dev).transpose(0, 2, 1, 3).reshape(SBLK)
    own_blocks = row_index * (local_rows // BS) + jnp.arange(local_rows // BS, dtype=jnp.int32)
    block_ids = jnp.arange(group_blocks, dtype=jnp.int32)
    compact = gathered.reshape(SBLK, -1, lanes)
    local_block = blocks_gathered - col_index * group_blocks
    hits = local_block[None, :] == block_ids[:, None]
    present = jnp.any(hits, axis=1)
    rank = jnp.cumsum(present.astype(jnp.int32)) - 1
    slot_ids = jnp.arange(CAP, dtype=jnp.int32)
    slot_of = present[None, :] & (rank[None, :] == slot_ids[:, None])
    picker = jnp.dot(slot_of.astype(jnp.float32), hits.astype(jnp.float32)).astype(jnp.bfloat16)
    slot_block = jnp.sum(jnp.where(slot_of, block_ids[None, :], 0), axis=1)
    picked = (
        jnp.einsum("jp,prl->jrl", picker, compact, preferred_element_type=jnp.float32)
        .astype(jnp.bfloat16)
        .reshape(CAP * BS, local_width)
    )
    anc_kept = jnp.take(anc_inv.reshape(local_rows, group_blocks, BS), slot_block, axis=1).reshape(local_rows, CAP * BS)
    expanded = lax.all_gather(lax.all_gather(picked, "x", axis=1, tiled=True), "zl", axis=1, tiled=True)
    width = expanded.shape[1]
    chunk = width // (n_y * n_zh * n_c)
    rhs = expanded.reshape(-1, n_y, n_zh, n_c, chunk)
    partial_value = jnp.einsum("mk,kyzcn->yczmn", anc_kept, rhs, preferred_element_type=jnp.float32)
    partial_value = partial_value.reshape(n_y * n_c, n_zh, local_rows, chunk)
    halves = lax.psum_scatter(partial_value, ("y", "c"), scatter_dimension=0, tiled=True)[0]
    mine = lax.dynamic_index_in_dim(halves, zh_index, 0, keepdims=False)
    other = lax.dynamic_index_in_dim(halves, 1 - zh_index, 0, keepdims=False)
    summed = mine + lax.ppermute(other, "zh", [(0, 1), (1, 0)])
    member = jnp.any(blocks_of[None, :] == own_blocks[:, None], axis=1)
    row_mask = jnp.repeat(member, BS)
    results = [jnp.where(row_mask[:, None], -summed, jnp.zeros_like(summed))]
    return jnp.stack(results)


def solution(mesh):
    rows, cols = mesh.shape["row"], mesh.shape["col"]
    fine = Mesh(mesh.devices.reshape(rows // 4, 4, cols // 4, 2, 2), ("zl", "x", "y", "zh", "c"))
    in_specs = (P(ROW, COL), P(None, COL, ROW), P())
    out_specs = P(None, ROW, COL)
    return jax.shard_map(body, mesh=fine, in_specs=in_specs, out_specs=out_specs, check_vma=False)
```

```python
import jax
import jax.numpy as jnp
from jax import lax
from jax.sharding import Mesh, PartitionSpec as P

BS = 128
SBLK = 96
CAP = 7
ROW = ("zl", "x")
COL = ("y", "zh", "c")


def body(anc_inv, panel, structure):
    n_y, n_zh, n_c = lax.axis_size("y"), lax.axis_size("zh"), lax.axis_size("c")
    col_index = lax.axis_index(COL)
    row_index = lax.axis_index(ROW)
    zh_index = lax.axis_index("zh")
    local_rows, local_cols = anc_inv.shape
    group_blocks = local_cols // BS
    local_width = panel.shape[2]
    per_dev = panel.shape[1] // BS
    lanes = BS
    dense = panel[0].reshape(-1, lanes)
    gathered = lax.all_gather(dense, ("y", "c"), axis=0, tiled=True)
    blocks_of = structure[0]
    by_col = blocks_of.reshape(n_y, n_zh, n_c, per_dev)
    blocks_half = lax.dynamic_index_in_dim(by_col, zh_index, 1, False).reshape(-1)
    own_blocks = row_index * (local_rows // BS) + jnp.arange(local_rows // BS, dtype=jnp.int32)
    block_ids = jnp.arange(group_blocks, dtype=jnp.int32)
    compact = gathered.reshape(blocks_half.shape[0], -1, lanes)
    same_group = (blocks_half[:, None] // group_blocks) == (blocks_of[None, :] // group_blocks)
    slot = jnp.sum(same_group & (blocks_of[None, :] < blocks_half[:, None]), axis=1)
    slot_ids = jnp.arange(CAP, dtype=jnp.int32)
    partner_col = col_index + (1 - 2 * zh_index) * n_c

    def pick(group):
        chosen = ((blocks_half // group_blocks)[None, :] == group) & (slot[None, :] == slot_ids[:, None])
        return jnp.einsum(
            "jp,prl->jrl", chosen.astype(jnp.bfloat16), compact, preferred_element_type=jnp.float32
        ).astype(jnp.bfloat16)

    from_partner = lax.ppermute(pick(partner_col), "zh", [(0, 1), (1, 0)])
    picked = (pick(col_index) + from_partner).reshape(CAP * BS, local_width)
    local_block = blocks_of - col_index * group_blocks
    hits = local_block[None, :] == block_ids[:, None]
    present = jnp.any(hits, axis=1)
    rank = jnp.cumsum(present.astype(jnp.int32)) - 1
    slot_of = present[None, :] & (rank[None, :] == slot_ids[:, None])
    slot_block = jnp.sum(jnp.where(slot_of, block_ids[None, :], 0), axis=1)
    anc_kept = jnp.take(anc_inv.reshape(local_rows, group_blocks, BS), slot_block, axis=1).reshape(local_rows, CAP * BS)
    expanded = lax.all_gather(lax.all_gather(picked, "x", axis=1, tiled=True), "zl", axis=1, tiled=True)
    width = expanded.shape[1]
    chunk = width // (n_y * n_zh * n_c)
    rhs = expanded.reshape(-1, n_y, n_zh, n_c, chunk)
    partial_value = jnp.einsum("mk,kyzcn->yczmn", anc_kept, rhs, preferred_element_type=jnp.float32)
    partial_value = partial_value.reshape(n_y * n_c, n_zh, local_rows, chunk)
    halves = lax.psum_scatter(partial_value, ("y", "c"), scatter_dimension=0, tiled=True)[0]
    mine = lax.dynamic_index_in_dim(halves, zh_index, 0, keepdims=False)
    other = lax.dynamic_index_in_dim(halves, 1 - zh_index, 0, keepdims=False)
    summed = mine + lax.ppermute(other, "zh", [(0, 1), (1, 0)])
    member = jnp.any(blocks_of[None, :] == own_blocks[:, None], axis=1)
    row_mask = jnp.repeat(member, BS)
    results = [jnp.where(row_mask[:, None], -summed, jnp.zeros_like(summed))]
    return jnp.stack(results)


def solution(mesh):
    rows, cols = mesh.shape["row"], mesh.shape["col"]
    fine = Mesh(mesh.devices.reshape(rows // 4, 4, cols // 4, 2, 2), ("zl", "x", "y", "zh", "c"))
    in_specs = (P(ROW, COL), P(None, COL, ROW), P())
    out_specs = P(None, ROW, COL)
    return jax.shard_map(body, mesh=fine, in_specs=in_specs, out_specs=out_specs, check_vma=False)
```

```python
import jax
import jax.numpy as jnp
from jax import lax
from jax.sharding import Mesh, PartitionSpec as P

BS = 128
SBLK = 96
CAP = 7
ROW = ("zl", "x")
COL = ("y", "zh", "c")


def body(anc_inv, panel, structure):
    n_y, n_zh, n_c = lax.axis_size("y"), lax.axis_size("zh"), lax.axis_size("c")
    col_index = lax.axis_index(COL)
    row_index = lax.axis_index(ROW)
    zh_index = lax.axis_index("zh")
    local_rows, local_cols = anc_inv.shape
    group_blocks = local_cols // BS
    local_width = panel.shape[2]
    per_dev = panel.shape[1] // BS
    lanes = BS
    dense = panel[0].reshape(-1, lanes)
    gathered = lax.all_gather(dense, ("y", "c"), axis=0, tiled=True)
    blocks_of = structure[0]
    by_col = blocks_of.reshape(n_y, n_zh, n_c, per_dev)
    blocks_half = lax.dynamic_index_in_dim(by_col, zh_index, 1, False).reshape(-1)
    own_blocks = row_index * (local_rows // BS) + jnp.arange(local_rows // BS, dtype=jnp.int32)
    block_ids = jnp.arange(group_blocks, dtype=jnp.int32)
    compact = gathered.reshape(blocks_half.shape[0], -1, lanes)
    same_group = (blocks_half[:, None] // group_blocks) == (blocks_of[None, :] // group_blocks)
    slot = jnp.sum(same_group & (blocks_of[None, :] < blocks_half[:, None]), axis=1)
    slot_ids = jnp.arange(CAP, dtype=jnp.int32)
    partner_col = col_index + (1 - 2 * zh_index) * n_c

    def pick(group):
        chosen = ((blocks_half // group_blocks)[None, :] == group) & (slot[None, :] == slot_ids[:, None])
        return jnp.einsum(
            "jp,prl->jrl", chosen.astype(jnp.bfloat16), compact, preferred_element_type=jnp.float32
        ).astype(jnp.bfloat16)

    both = lax.all_gather(pick(partner_col), "zh", axis=0, tiled=False)
    from_partner = lax.dynamic_index_in_dim(both, 1 - zh_index, 0, keepdims=False)
    picked = (pick(col_index) + from_partner).reshape(CAP * BS, local_width)
    local_block = blocks_of - col_index * group_blocks
    hits = local_block[None, :] == block_ids[:, None]
    present = jnp.any(hits, axis=1)
    rank = jnp.cumsum(present.astype(jnp.int32)) - 1
    slot_of = present[None, :] & (rank[None, :] == slot_ids[:, None])
    slot_block = jnp.sum(jnp.where(slot_of, block_ids[None, :], 0), axis=1)
    anc_kept = jnp.take(anc_inv.reshape(local_rows, group_blocks, BS), slot_block, axis=1).reshape(local_rows, CAP * BS)
    expanded = lax.all_gather(lax.all_gather(picked, "x", axis=1, tiled=True), "zl", axis=1, tiled=True)
    width = expanded.shape[1]
    chunk = width // (n_y * n_zh * n_c)
    rhs = expanded.reshape(-1, n_y, n_zh, n_c, chunk)
    partial_value = jnp.einsum("mk,kyzcn->yczmn", anc_kept, rhs, preferred_element_type=jnp.float32)
    partial_value = partial_value.reshape(n_y * n_c, n_zh, local_rows, chunk)
    halves = lax.psum_scatter(partial_value, ("y", "c"), scatter_dimension=0, tiled=True)[0]
    mine = lax.dynamic_index_in_dim(halves, zh_index, 0, keepdims=False)
    other = lax.dynamic_index_in_dim(halves, 1 - zh_index, 0, keepdims=False)
    summed = mine + lax.ppermute(other, "zh", [(0, 1), (1, 0)])
    member = jnp.any(blocks_of[None, :] == own_blocks[:, None], axis=1)
    row_mask = jnp.repeat(member, BS)
    results = [jnp.where(row_mask[:, None], -summed, jnp.zeros_like(summed))]
    return jnp.stack(results)


def solution(mesh):
    rows, cols = mesh.shape["row"], mesh.shape["col"]
    fine = Mesh(mesh.devices.reshape(rows // 4, 4, cols // 4, 2, 2), ("zl", "x", "y", "zh", "c"))
    in_specs = (P(ROW, COL), P(None, COL, ROW), P())
    out_specs = P(None, ROW, COL)
    return jax.shard_map(body, mesh=fine, in_specs=in_specs, out_specs=out_specs, check_vma=False)
```

```python
import jax
import jax.numpy as jnp
from jax import lax
from jax.sharding import Mesh, PartitionSpec as P

BS = 128
SBLK = 96
CAP = 7
ROW = ("zl", "x")
COL = ("y", "zh", "c")


def body(anc_inv, panel, structure):
    n_y, n_zh, n_c = lax.axis_size("y"), lax.axis_size("zh"), lax.axis_size("c")
    col_index = lax.axis_index(COL)
    row_index = lax.axis_index(ROW)
    zh_index = lax.axis_index("zh")
    local_rows, local_cols = anc_inv.shape
    group_blocks = local_cols // BS
    local_width = panel.shape[2]
    per_dev = panel.shape[1] // BS
    lanes = BS
    dense = panel[0].reshape(-1, lanes)
    gathered = lax.all_gather(dense, ("y", "c"), axis=0, tiled=True)
    blocks_of = structure[0]
    by_col = blocks_of.reshape(n_y, n_zh, n_c, per_dev)
    blocks_half = lax.dynamic_index_in_dim(by_col, zh_index, 1, False).reshape(-1)
    own_blocks = row_index * (local_rows // BS) + jnp.arange(local_rows // BS, dtype=jnp.int32)
    block_ids = jnp.arange(group_blocks, dtype=jnp.int32)
    compact = gathered.reshape(blocks_half.shape[0], -1, lanes)
    same_group = (blocks_half[:, None] // group_blocks) == (blocks_of[None, :] // group_blocks)
    slot = jnp.sum(same_group & (blocks_of[None, :] < blocks_half[:, None]), axis=1)
    slot_ids = jnp.arange(CAP, dtype=jnp.int32)
    partner_col = col_index + (1 - 2 * zh_index) * n_c

    def pick(group):
        chosen = ((blocks_half // group_blocks)[None, :] == group) & (slot[None, :] == slot_ids[:, None])
        return jnp.einsum(
            "jp,prl->jrl", chosen.astype(jnp.bfloat16), compact, preferred_element_type=jnp.float32
        ).astype(jnp.bfloat16)

    both = lax.all_gather(pick(partner_col), "zh", axis=0, tiled=False)
    from_partner = lax.dynamic_index_in_dim(both, 1 - zh_index, 0, keepdims=False)
    picked = (pick(col_index) + from_partner).reshape(CAP * BS, local_width)
    local_block = blocks_of - col_index * group_blocks
    hits = local_block[None, :] == block_ids[:, None]
    present = jnp.any(hits, axis=1)
    rank = jnp.cumsum(present.astype(jnp.int32)) - 1
    slot_of = present[None, :] & (rank[None, :] == slot_ids[:, None])
    slot_block = jnp.sum(jnp.where(slot_of, block_ids[None, :], 0), axis=1)
    anc_kept = jnp.take(anc_inv.reshape(local_rows, group_blocks, BS), slot_block, axis=1).reshape(local_rows, CAP * BS)
    expanded = lax.all_gather(lax.all_gather(picked, "x", axis=1, tiled=True), "zl", axis=1, tiled=True)
    width = expanded.shape[1]
    chunk = width // (n_y * n_zh * n_c)
    rhs = expanded.reshape(-1, n_y, n_zh, n_c, chunk)
    partial_value = jnp.einsum("mk,kyzcn->yczmn", anc_kept, rhs, preferred_element_type=jnp.float32)
    partial_value = partial_value.reshape(n_y * n_c, n_zh, local_rows, chunk)
    halves = lax.psum_scatter(partial_value, ("y", "c"), scatter_dimension=0, tiled=True)[0]
    mine = lax.dynamic_index_in_dim(halves, zh_index, 0, keepdims=False)
    other = lax.dynamic_index_in_dim(halves, 1 - zh_index, 0, keepdims=False)
    both_halves = lax.all_gather(other, "zh", axis=0, tiled=False)
    summed = mine + lax.dynamic_index_in_dim(both_halves, 1 - zh_index, 0, keepdims=False)
    member = jnp.any(blocks_of[None, :] == own_blocks[:, None], axis=1)
    row_mask = jnp.repeat(member, BS)
    results = [jnp.where(row_mask[:, None], -summed, jnp.zeros_like(summed))]
    return jnp.stack(results)


def solution(mesh):
    rows, cols = mesh.shape["row"], mesh.shape["col"]
    fine = Mesh(mesh.devices.reshape(rows // 4, 4, cols // 4, 2, 2), ("zl", "x", "y", "zh", "c"))
    in_specs = (P(ROW, COL), P(None, COL, ROW), P())
    out_specs = P(None, ROW, COL)
    return jax.shard_map(body, mesh=fine, in_specs=in_specs, out_specs=out_specs, check_vma=False)
```

```python
import jax
import jax.numpy as jnp
from jax import lax
from jax.sharding import Mesh, PartitionSpec as P

BS = 128
SBLK = 96
CAP = 7
ROW = ("zl", "x")
COL = ("y", "zh", "c")


def body(anc_inv, panel, structure):
    n_y, n_zh, n_c = lax.axis_size("y"), lax.axis_size("zh"), lax.axis_size("c")
    col_index = lax.axis_index(COL)
    row_index = lax.axis_index(ROW)
    zh_index = lax.axis_index("zh")
    local_rows, local_cols = anc_inv.shape
    group_blocks = local_cols // BS
    local_width = panel.shape[2]
    per_dev = panel.shape[1] // BS
    lanes = BS
    dense = panel[0].reshape(-1, lanes)
    gathered = lax.all_gather(dense, ("y", "c"), axis=0, tiled=True)
    blocks_of = structure[0]
    by_col = blocks_of.reshape(n_y, n_zh, n_c, per_dev)
    blocks_half = lax.dynamic_index_in_dim(by_col, zh_index, 1, False).reshape(-1)
    own_blocks = row_index * (local_rows // BS) + jnp.arange(local_rows // BS, dtype=jnp.int32)
    block_ids = jnp.arange(group_blocks, dtype=jnp.int32)
    compact = gathered.reshape(blocks_half.shape[0], -1, lanes)
    same_group = (blocks_half[:, None] // group_blocks) == (blocks_of[None, :] // group_blocks)
    slot = jnp.sum(same_group & (blocks_of[None, :] < blocks_half[:, None]), axis=1)
    slot_ids = jnp.arange(CAP, dtype=jnp.int32)
    partner_col = col_index + (1 - 2 * zh_index) * n_c

    def pick(group):
        chosen = ((blocks_half // group_blocks)[None, :] == group) & (slot[None, :] == slot_ids[:, None])
        return jnp.einsum(
            "jp,prl->jrl", chosen.astype(jnp.bfloat16), compact, preferred_element_type=jnp.float32
        ).astype(jnp.bfloat16)

    both = lax.all_gather(pick(partner_col), "zh", axis=0, tiled=False)
    from_partner = lax.dynamic_index_in_dim(both, 1 - zh_index, 0, keepdims=False)
    picked = pick(col_index) + from_partner
    local_block = blocks_of - col_index * group_blocks
    hits = local_block[None, :] == block_ids[:, None]
    present = jnp.any(hits, axis=1)
    rank = jnp.cumsum(present.astype(jnp.int32)) - 1
    slot_of = present[None, :] & (rank[None, :] == slot_ids[:, None])
    slot_block = jnp.sum(jnp.where(slot_of, block_ids[None, :], 0), axis=1)
    anc_kept = jnp.take(anc_inv.reshape(local_rows, group_blocks, BS), slot_block, axis=1).reshape(local_rows, CAP * BS)
    n_x = lax.axis_size("x")
    over_x = lax.all_gather(picked, "x", axis=0).reshape(n_x, CAP * BS, local_width)
    over_x = over_x.transpose(1, 0, 2).reshape(CAP * BS, n_x * local_width)
    expanded = lax.all_gather(over_x, "zl", axis=1, tiled=True)
    width = expanded.shape[1]
    chunk = width // (n_y * n_zh * n_c)
    rhs = expanded.reshape(-1, n_y, n_zh, n_c, chunk)
    partial_value = jnp.einsum("mk,kyzcn->yczmn", anc_kept, rhs, preferred_element_type=jnp.float32)
    partial_value = partial_value.reshape(n_y * n_c, n_zh, local_rows, chunk)
    halves = lax.psum_scatter(partial_value, ("y", "c"), scatter_dimension=0, tiled=True)[0]
    mine = lax.dynamic_index_in_dim(halves, zh_index, 0, keepdims=False)
    other = lax.dynamic_index_in_dim(halves, 1 - zh_index, 0, keepdims=False)
    both_halves = lax.all_gather(other, "zh", axis=0, tiled=False)
    summed = mine + lax.dynamic_index_in_dim(both_halves, 1 - zh_index, 0, keepdims=False)
    member = jnp.any(blocks_of[None, :] == own_blocks[:, None], axis=1)
    row_mask = jnp.repeat(member, BS)
    results = [jnp.where(row_mask[:, None], -summed, jnp.zeros_like(summed))]
    return jnp.stack(results)


def solution(mesh):
    rows, cols = mesh.shape["row"], mesh.shape["col"]
    fine = Mesh(mesh.devices.reshape(rows // 4, 4, cols // 4, 2, 2), ("zl", "x", "y", "zh", "c"))
    in_specs = (P(ROW, COL), P(None, COL, ROW), P())
    out_specs = P(None, ROW, COL)
    return jax.shard_map(body, mesh=fine, in_specs=in_specs, out_specs=out_specs, check_vma=False)
```
